256 devices in a mesh: dp: 32 (over z_hi, y, core), mp: 8 (over x, z_lo).
Axes of the slice: x: 4, y: 4, z: 8 (z_hi: 4, z_lo: 2; z = z_hi * 2 + z_lo), core: 2. Of those that a mesh axis runs over, the one named last changes fastest.
Arguments:
- activations: bfloat16 [2, 64, 384, 14336], P(None, 'dp', None, 'mp'), may hold values from -6 to 6
- out_grads: bfloat16 [2, 64, 384, 4096], P(None, 'dp', None, 'mp'), may hold values from -6 to 6
- proj_in: bfloat16 [14336, 64], P('mp'), may hold values from -0.046875 to 0.046875
- proj_out: bfloat16 [4096, 64], P('mp'), may hold values from -0.09375 to 0.09375
- store: bfloat16 [2, 65536, 4096], P(None, ('dp', 'mp')), may hold values from -0.09375 to 0.09375
- ckpt_rate: float32 [2], replicated, may hold values from 0.5 to 2
- store_group: int32 [65536], P(('dp', 'mp')), may hold values from 0 to 15
Outputs:
- scores: float32 [64, 65536], P(None, ('dp', 'mp'))
- group_scores: float32 [64, 16], replicated
The draws below stay inside these ranges and needn't reach their ends.
All inputs are finite; a program needn't handle non-finite values.
Results may differ from the reference program's by a relative error of at most 0.005.
Values may be sent and summed in bfloat16 or wider, within the bound.
No kernel may reach another device: no remote copies, remote signals or barrier semaphores. Data moves between devices by JAX's collectives and lax.ppermute only.
A program may use at most 64 MiB of HBM per device.

```python
import math
import jax
import jax.numpy as jnp
from jax import lax

D = 4096
FF = 14336
RANK = 64
SEQ = 384
GROUPS = 16
EXAMPLES = 64
STORE = 65536


def plant(values, rng, least, largest):
    shape = values.shape
    spot = [jax.random.randint(jax.random.fold_in(rng, axis), (), 0, shape[axis]) for axis in range(len(shape))]
    values = values.at[tuple(spot)].set(least)
    longest = shape.index(max(shape))
    spot[longest] = (spot[longest] + 1) % shape[longest]
    return values.at[tuple(spot)].set(largest)


def block_levels(own_key, extent, cuts, low, high):
    def one(axis_at, parts):
        steps = jax.random.uniform(jax.random.fold_in(jax.random.fold_in(own_key, 6), axis_at), (parts,), jnp.float32, low / len(cuts), high / len(cuts))
        return jnp.repeat(jnp.exp(steps), extent[axis_at] // parts).reshape((-1,) + (1,) * (len(extent) - axis_at - 1))

    factor_of = one(*cuts[0])
    for cut in cuts[1:]:
        factor_of = factor_of * one(*cut)
    return factor_of


def bell_draw(key, shape, scale, bound, cuts=(), kind=jnp.bfloat16):
    entries = scale * jax.random.normal(key, shape, jnp.float32)
    if cuts:
        entries = entries * block_levels(key, shape, cuts, -0.22, 0.18)
    return jnp.clip(entries, -bound, bound).astype(kind)


def setup_inputs(seed: int = 0) -> dict:
    arg_keys = jax.random.split(jax.random.key(seed), 8)
    return {
        "activations": bell_draw(arg_keys[0], (2, EXAMPLES, SEQ, FF), 1.0, 6.0, ((1, 32), (3, 8))),
        "out_grads": bell_draw(arg_keys[1], (2, EXAMPLES, SEQ, D), 1.0, 6.0, ((1, 32), (3, 8))),
        "proj_in": bell_draw(arg_keys[2], (FF, RANK), FF ** -0.5, 0.046875, ((0, 8),)),
        "proj_out": bell_draw(arg_keys[3], (D, RANK), D ** -0.5, 0.09375, ((0, 8),)),
        "store": bell_draw(arg_keys[4], (2, STORE, RANK * RANK), (RANK * RANK) ** -0.5, 0.09375, ((1, 256),)),
        "ckpt_rate": jnp.clip(jnp.exp(jax.random.uniform(arg_keys[5], (2,), jnp.float32, math.log(0.5), math.log(2.0))), 0.5, 2.0),
        "store_group": plant(jax.random.randint(arg_keys[6], (STORE,), 0, GROUPS), jax.random.fold_in(arg_keys[6], 1), 0, GROUPS - 1).astype(jnp.int32),
    }


def reference(activations, out_grads, proj_in, proj_out, store, ckpt_rate, store_group):
    queries = []
    for ckpt in range(2):
        flat_act = activations[ckpt].reshape(EXAMPLES * SEQ, FF)
        flat_grad = out_grads[ckpt].reshape(EXAMPLES * SEQ, D)
        low_in = jnp.dot(flat_act, proj_in, preferred_element_type=jnp.float32).astype(jnp.bfloat16)
        low_grad = jnp.dot(flat_grad, proj_out, preferred_element_type=jnp.float32).astype(jnp.bfloat16)
        low_in = low_in.reshape(EXAMPLES, SEQ, RANK).astype(jnp.float32)
        low_grad = low_grad.reshape(EXAMPLES, SEQ, RANK).astype(jnp.float32)
        outer = jnp.einsum('esa,esb->eab', low_in, low_grad) / jnp.sqrt(jnp.float32(SEQ))
        queries.append(outer.reshape(EXAMPLES, RANK * RANK).astype(jnp.bfloat16))
    scores = ckpt_rate[0] * jnp.dot(queries[0], store[0].T, preferred_element_type=jnp.float32)
    scores = scores + ckpt_rate[1] * jnp.dot(queries[1], store[1].T, preferred_element_type=jnp.float32)
    member = (store_group[:, None] == jnp.arange(GROUPS, dtype=jnp.int32)[None, :]).astype(jnp.float32)
    totals = jnp.dot(scores, member, precision=lax.Precision.HIGHEST)
    group_scores = totals / jnp.sqrt(jnp.float32(STORE) / jnp.float32(GROUPS))
    return (scores, group_scores)
```

```python
import jax
import jax.numpy as jnp
from jax import lax
from jax.sharding import PartitionSpec as P

GROUPS = 16


def _bits(n):
    return n.bit_length() - 1


def _swap(axis, n, bit):
    return [(i, i ^ (1 << bit)) for i in range(n)]


def _halving_sum(x, axis, n, dim):
    me = lax.axis_index(axis)
    for bit in reversed(range(_bits(n))):
        half = x.shape[dim] // 2
        upper = (me >> bit) & 1
        keep = lax.dynamic_slice_in_dim(x, upper * half, half, axis=dim)
        send = lax.dynamic_slice_in_dim(x, (1 - upper) * half, half, axis=dim)
        x = keep + lax.ppermute(send, axis, _swap(axis, n, bit))
    return x


def _doubling_gather(x, steps):
    for axis, n, bit in steps:
        upper = ((lax.axis_index(axis) >> bit) & 1) == 1
        other = lax.ppermute(x, axis, _swap(axis, n, bit))
        x = jnp.where(upper, jnp.stack([other, x]), jnp.stack([x, other]))
    return x


def _butterfly_sum(x, steps):
    for axis, n, bit in steps:
        x = x + lax.ppermute(x, axis, _swap(axis, n, bit))
    return x


def shards(activations, out_grads, proj_in, proj_out, store, ckpt_rate, store_group):
    n_dp = lax.axis_size("dp")
    n_mp = lax.axis_size("mp")
    rank = proj_in.shape[1]
    seq_len = activations.shape[2]
    ex_local = activations.shape[1]
    part_in = jnp.einsum("cesf,fr->cesr", activations, proj_in, preferred_element_type=jnp.float32)
    part_out = jnp.einsum("cesf,fr->cesr", out_grads, proj_out, preferred_element_type=jnp.float32)
    stacked = jnp.concatenate([part_in, part_out], axis=3)
    summed = _halving_sum(stacked, "mp", n_mp, 2)
    low_in = summed[..., :rank].astype(jnp.bfloat16)
    low_grad = summed[..., rank:].astype(jnp.bfloat16)
    outer = jnp.einsum("cesa,cesb->ecab", low_in, low_grad, preferred_element_type=jnp.float32)
    outer = outer.reshape(ex_local, 2, rank * rank)
    outer = _halving_sum(outer, "mp", n_mp, 2)
    query = (outer / jnp.sqrt(jnp.float32(seq_len))).astype(jnp.bfloat16)
    dp_bits, mp_bits = _bits(n_dp), _bits(n_mp)
    order = [("dp", n_dp, b) for b in reversed(range(1, dp_bits))]
    order += [("mp", n_mp, b) for b in reversed(range(mp_bits))]
    order += [("dp", n_dp, 0)]
    gathered = _doubling_gather(query, order)
    steps = len(order)
    lead = {(a, b): steps - 1 - i for i, (a, _, b) in enumerate(order)}
    dp_axes = [lead[("dp", b)] for b in reversed(range(dp_bits))]
    mp_axes = [lead[("mp", b)] for b in reversed(range(mp_bits))]
    perm = dp_axes + [steps] + [steps + 1] + mp_axes + [steps + 2]
    piece = jnp.transpose(gathered, perm).reshape(n_dp * ex_local, 2, rank * rank)
    first = jnp.einsum("qk,rk->qr", piece[:, 0], store[0], preferred_element_type=jnp.float32)
    second = jnp.einsum("qk,rk->qr", piece[:, 1], store[1], preferred_element_type=jnp.float32)
    scores = ckpt_rate[0] * first + ckpt_rate[1] * second
    member = (store_group[:, None] == jnp.arange(GROUPS, dtype=jnp.int32)[None, :]).astype(
        jnp.float32
    )
    partial_totals = jnp.dot(scores, member, precision=lax.Precision.HIGHEST)
    reduce_order = [("mp", n_mp, b) for b in range(mp_bits)] + [("dp", n_dp, b) for b in range(dp_bits)]
    totals = _butterfly_sum(partial_totals, reduce_order)
    store_rows = store.shape[1] * n_dp * n_mp
    group_scores = totals / jnp.sqrt(jnp.float32(store_rows) / jnp.float32(GROUPS))
    return (scores, group_scores)


def solution(mesh):
    placed = (
        P(None, "dp", None, "mp"),
        P(None, "dp", None, "mp"),
        P("mp", None),
        P("mp", None),
        P(None, ("dp", "mp"), None),
        P(),
        P(("dp", "mp")),
    )
    return jax.shard_map(
        shards, mesh=mesh, in_specs=placed, out_specs=(P(None, ("dp", "mp")), P()), check_vma=False
    )
```

```python
import jax
import jax.numpy as jnp
from jax import lax
from jax.sharding import PartitionSpec as P

GROUPS = 16


def _bits(n):
    return n.bit_length() - 1


def _swap(n, bit):
    return [(i, i ^ (1 << bit)) for i in range(n)]


def _halving_sum(x, axis, n, dim, order):
    me = lax.axis_index(axis)
    for bit in order:
        half = x.shape[dim] // 2
        upper = (me >> bit) & 1
        keep = lax.dynamic_slice_in_dim(x, upper * half, half, axis=dim)
        send = lax.dynamic_slice_in_dim(x, (1 - upper) * half, half, axis=dim)
        x = keep + lax.ppermute(send, axis, _swap(n, bit))
    return x


def _butterfly_sum(x, axis, n, order):
    for bit in order:
        x = x + lax.ppermute(x, axis, _swap(n, bit))
    return x


def _join(x, other, upper, dim):
    return jnp.where(upper, jnp.concatenate([other, x], dim), jnp.concatenate([x, other], dim))


def shards(activations, out_grads, proj_in, proj_out, store, ckpt_rate, store_group):
    n_dp = lax.axis_size("dp")
    n_mp = lax.axis_size("mp")
    dp_bits, mp_bits = _bits(n_dp), _bits(n_mp)
    rank = proj_in.shape[1]
    seq_len = activations.shape[2]
    ex_local = activations.shape[1]
    near_first = list(range(mp_bits))

    member = (store_group[:, None] == jnp.arange(GROUPS, dtype=jnp.int32)[None, :]).astype(
        jnp.bfloat16
    )
    group_rows = jnp.einsum("rg,crk->cgk", member, store, preferred_element_type=jnp.float32)
    group_rows = _halving_sum(group_rows, "mp", n_mp, 2, near_first)
    group_rows = _butterfly_sum(group_rows, "dp", n_dp, list(range(dp_bits)))

    part_in = jnp.einsum("cesf,fr->cesr", activations, proj_in, preferred_element_type=jnp.float32)
    part_out = jnp.einsum("cesf,fr->cesr", out_grads, proj_out, preferred_element_type=jnp.float32)
    stacked = jnp.concatenate([part_in, part_out], axis=3)
    summed = _halving_sum(stacked, "mp", n_mp, 2, near_first)
    low_in = summed[..., :rank].astype(jnp.bfloat16)
    low_grad = summed[..., rank:].astype(jnp.bfloat16)
    outer = jnp.einsum("cesa,cesb->ecab", low_in, low_grad, preferred_element_type=jnp.float32)
    outer = outer.reshape(ex_local, 2, rank * rank)
    outer = _halving_sum(outer, "mp", n_mp, 2, near_first)
    query = (outer / jnp.sqrt(jnp.float32(seq_len))).astype(jnp.bfloat16)

    in_slice = jnp.einsum(
        "eck,cgk->ecg", query.astype(jnp.float32), group_rows, precision=lax.Precision.HIGHEST
    )
    group_part = ckpt_rate[0] * in_slice[:, 0] + ckpt_rate[1] * in_slice[:, 1]

    order = [("dp", b) for b in reversed(range(1, dp_bits))]
    order += [("mp", b) for b in reversed(range(mp_bits))]
    order += [("dp", 0)]
    piece, totals = query, group_part
    for axis, bit in order:
        n = n_dp if axis == "dp" else n_mp
        upper = ((lax.axis_index(axis) >> bit) & 1) == 1
        other = lax.ppermute(piece, axis, _swap(n, bit))
        other_totals = lax.ppermute(totals, axis, _swap(n, bit))
        if axis == "dp":
            piece = _join(piece, other, upper, 0)
            totals = _join(totals, other_totals, upper, 0)
        else:
            piece = _join(piece, other, upper, 2)
            totals = totals + other_totals
    first = jnp.einsum("qk,rk->qr", piece[:, 0], store[0], preferred_element_type=jnp.float32)
    second = jnp.einsum("qk,rk->qr", piece[:, 1], store[1], preferred_element_type=jnp.float32)
    scores = ckpt_rate[0] * first + ckpt_rate[1] * second

    def natural(x):
        x = x.reshape((2,) * dp_bits + (ex_local,) + x.shape[1:])
        perm = list(reversed(range(dp_bits))) + list(range(dp_bits, x.ndim))
        return jnp.transpose(x, perm).reshape((n_dp * ex_local,) + x.shape[dp_bits + 1 :])

    scores = natural(scores)
    store_rows = store.shape[1] * n_dp * n_mp
    group_scores = natural(totals) / jnp.sqrt(jnp.float32(store_rows) / jnp.float32(GROUPS))
    return (scores, group_scores)


def solution(mesh):
    placed = (
        P(None, "dp", None, "mp"),
        P(None, "dp", None, "mp"),
        P("mp", None),
        P("mp", None),
        P(None, ("dp", "mp"), None),
        P(),
        P(("dp", "mp")),
    )
    return jax.shard_map(
        shards, mesh=mesh, in_specs=placed, out_specs=(P(None, ("dp", "mp")), P()), check_vma=False
    )
```

```python
import jax
import jax.numpy as jnp
from jax import lax
from jax.sharding import PartitionSpec as P

GROUPS = 16


def _bits(n):
    return n.bit_length() - 1


def _swap(n, bit):
    return [(i, i ^ (1 << bit)) for i in range(n)]


def _halving_sum(x, axis, n, dim, order):
    me = lax.axis_index(axis)
    for bit in order:
        half = x.shape[dim] // 2
        upper = (me >> bit) & 1
        keep = lax.dynamic_slice_in_dim(x, upper * half, half, axis=dim)
        send = lax.dynamic_slice_in_dim(x, (1 - upper) * half, half, axis=dim)
        x = keep + lax.ppermute(send, axis, _swap(n, bit))
    return x


def _butterfly_sum(x, axis, n, order):
    for bit in order:
        x = x + lax.ppermute(x, axis, _swap(n, bit))
    return x


def _join(x, other, upper, dim):
    return jnp.where(upper, jnp.concatenate([other, x], dim), jnp.concatenate([x, other], dim))


def _doubling_gather(x, axis, n, dim, order):
    me = lax.axis_index(axis)
    for bit in order:
        upper = ((me >> bit) & 1) == 1
        x = _join(x, lax.ppermute(x, axis, _swap(n, bit)), upper, dim)
    return x


def shards(activations, out_grads, proj_in, proj_out, store, ckpt_rate, store_group):
    n_dp = lax.axis_size("dp")
    n_mp = lax.axis_size("mp")
    dp_bits, mp_bits = _bits(n_dp), _bits(n_mp)
    rank = proj_in.shape[1]
    seq_len = activations.shape[2]
    ex_local = activations.shape[1]

    part_in = jnp.einsum("cesf,fr->cesr", activations, proj_in, preferred_element_type=jnp.float32)
    part_out = jnp.einsum("cesf,fr->cesr", out_grads, proj_out, preferred_element_type=jnp.float32)
    stacked = jnp.concatenate([part_in, part_out], axis=3)
    summed = _halving_sum(stacked, "mp", n_mp, 2, list(range(mp_bits)))
    low = _doubling_gather(summed.astype(jnp.bfloat16), "mp", n_mp, 2, list(reversed(range(mp_bits))))
    outer = jnp.einsum(
        "cesa,cesb->ecab", low[..., :rank], low[..., rank:], preferred_element_type=jnp.float32
    )
    outer = outer.reshape(ex_local, 2, rank * rank)
    query = (outer / jnp.sqrt(jnp.float32(seq_len))).astype(jnp.bfloat16)
    piece = _doubling_gather(query, "dp", n_dp, 0, list(reversed(range(dp_bits))))
    first = jnp.einsum("qk,rk->qr", piece[:, 0], store[0], preferred_element_type=jnp.float32)
    second = jnp.einsum("qk,rk->qr", piece[:, 1], store[1], preferred_element_type=jnp.float32)
    scores = ckpt_rate[0] * first + ckpt_rate[1] * second
    member = (store_group[:, None] == jnp.arange(GROUPS, dtype=jnp.int32)[None, :]).astype(
        jnp.float32
    )
    partial_totals = jnp.dot(scores, member, precision=lax.Precision.HIGHEST)
    totals = _butterfly_sum(partial_totals, "mp", n_mp, list(range(mp_bits)))
    totals = _butterfly_sum(totals, "dp", n_dp, list(range(dp_bits)))

    def natural(x):
        x = x.reshape((2,) * dp_bits + (ex_local,) + x.shape[1:])
        perm = list(reversed(range(dp_bits))) + list(range(dp_bits, x.ndim))
        return jnp.transpose(x, perm).reshape((n_dp * ex_local,) + x.shape[dp_bits + 1 :])

    scores = natural(scores)
    store_rows = store.shape[1] * n_dp * n_mp
    group_scores = natural(totals) / jnp.sqrt(jnp.float32(store_rows) / jnp.float32(GROUPS))
    return (scores, group_scores)


def solution(mesh):
    placed = (
        P(None, "dp", None, "mp"),
        P(None, "dp", None, "mp"),
        P("mp", None),
        P("mp", None),
        P(None, ("dp", "mp"), None),
        P(),
        P(("dp", "mp")),
    )
    return jax.shard_map(
        shards, mesh=mesh, in_specs=placed, out_specs=(P(None, ("dp", "mp")), P()), check_vma=False
    )
```

```python
import jax
import jax.numpy as jnp
from jax import lax
from jax.sharding import PartitionSpec as P

GROUPS = 16


def _bits(n):
    return n.bit_length() - 1


def _swap(n, bit):
    return [(i, i ^ (1 << bit)) for i in range(n)]


def _halving_sum(x, axis, n, dim, order):
    me = lax.axis_index(axis)
    for bit in order:
        half = x.shape[dim] // 2
        upper = (me >> bit) & 1
        keep = lax.dynamic_slice_in_dim(x, upper * half, half, axis=dim)
        send = lax.dynamic_slice_in_dim(x, (1 - upper) * half, half, axis=dim)
        x = keep + lax.ppermute(send, axis, _swap(n, bit))
    return x


def _butterfly_sum(x, axis, n, order):
    for bit in order:
        x = x + lax.ppermute(x, axis, _swap(n, bit))
    return x


def _join(x, other, upper, dim):
    return jnp.where(upper, jnp.concatenate([other, x], dim), jnp.concatenate([x, other], dim))


def _doubling_gather(x, axis, n, dim, order):
    me = lax.axis_index(axis)
    for bit in order:
        upper = ((me >> bit) & 1) == 1
        x = _join(x, lax.ppermute(x, axis, _swap(n, bit)), upper, dim)
    return x


def shards(activations, out_grads, proj_in, proj_out, store, ckpt_rate, store_group):
    n_dp = lax.axis_size("dp")
    n_mp = lax.axis_size("mp")
    dp_bits, mp_bits = _bits(n_dp), _bits(n_mp)
    rank = proj_in.shape[1]
    seq_len = activations.shape[2]
    ex_local = activations.shape[1]

    part_in = jnp.einsum("cesf,fr->cesr", activations, proj_in, preferred_element_type=jnp.float32)
    part_out = jnp.einsum("cesf,fr->cesr", out_grads, proj_out, preferred_element_type=jnp.float32)
    stacked = jnp.concatenate([part_in, part_out], axis=3)
    c, e, t, r = stacked.shape
    shares = lax.all_to_all(
        stacked.reshape(c, e, n_mp, t // n_mp, r), "mp", 2, 2, tiled=True
    )
    summed = shares.sum(2).astype(jnp.bfloat16)
    copies = jnp.broadcast_to(summed[:, :, None], (c, e, n_mp, t // n_mp, r))
    low = lax.all_to_all(copies, "mp", 2, 2, tiled=True).reshape(c, e, t, r)
    outer = jnp.einsum(
        "cesa,cesb->ecab", low[..., :rank], low[..., rank:], preferred_element_type=jnp.float32
    )
    outer = outer.reshape(ex_local, 2, rank * rank)
    query = (outer / jnp.sqrt(jnp.float32(seq_len))).astype(jnp.bfloat16)
    piece = _doubling_gather(query, "dp", n_dp, 0, list(reversed(range(dp_bits))))
    first = jnp.einsum("qk,rk->qr", piece[:, 0], store[0], preferred_element_type=jnp.float32)
    second = jnp.einsum("qk,rk->qr", piece[:, 1], store[1], preferred_element_type=jnp.float32)
    scores = ckpt_rate[0] * first + ckpt_rate[1] * second
    member = (store_group[:, None] == jnp.arange(GROUPS, dtype=jnp.int32)[None, :]).astype(
        jnp.float32
    )
    partial_totals = jnp.dot(scores, member, precision=lax.Precision.HIGHEST)
    totals = _butterfly_sum(partial_totals, "mp", n_mp, list(range(mp_bits)))
    totals = _butterfly_sum(totals, "dp", n_dp, list(range(dp_bits)))

    def natural(x):
        x = x.reshape((2,) * dp_bits + (ex_local,) + x.shape[1:])
        perm = list(reversed(range(dp_bits))) + list(range(dp_bits, x.ndim))
        return jnp.transpose(x, perm).reshape((n_dp * ex_local,) + x.shape[dp_bits + 1 :])

    scores = natural(scores)
    store_rows = store.shape[1] * n_dp * n_mp
    group_scores = natural(totals) / jnp.sqrt(jnp.float32(store_rows) / jnp.float32(GROUPS))
    return (scores, group_scores)


def solution(mesh):
    placed = (
        P(None, "dp", None, "mp"),
        P(None, "dp", None, "mp"),
        P("mp", None),
        P("mp", None),
        P(None, ("dp", "mp"), None),
        P(),
        P(("dp", "mp")),
    )
    return jax.shard_map(
        shards, mesh=mesh, in_specs=placed, out_specs=(P(None, ("dp", "mp")), P()), check_vma=False
    )
```

```python
import jax
import jax.numpy as jnp
from jax import lax
from jax.sharding import PartitionSpec as P

GROUPS = 16


def _bits(n):
    return n.bit_length() - 1


def _swap(n, bit):
    return [(i, i ^ (1 << bit)) for i in range(n)]


def _halving_sum(x, axis, n, dim, order):
    me = lax.axis_index(axis)
    for bit in order:
        half = x.shape[dim] // 2
        upper = (me >> bit) & 1
        keep = lax.dynamic_slice_in_dim(x, upper * half, half, axis=dim)
        send = lax.dynamic_slice_in_dim(x, (1 - upper) * half, half, axis=dim)
        x = keep + lax.ppermute(send, axis, _swap(n, bit))
    return x


def _butterfly_sum(x, axis, n, order):
    for bit in order:
        x = x + lax.ppermute(x, axis, _swap(n, bit))
    return x


def _join(x, other, upper, dim):
    return jnp.where(upper, jnp.concatenate([other, x], dim), jnp.concatenate([x, other], dim))


def _doubling_gather(x, axis, n, dim, order):
    me = lax.axis_index(axis)
    for bit in order:
        upper = ((me >> bit) & 1) == 1
        x = _join(x, lax.ppermute(x, axis, _swap(n, bit)), upper, dim)
    return x


def shards(activations, out_grads, proj_in, proj_out, store, ckpt_rate, store_group):
    n_dp = lax.axis_size("dp")
    n_mp = lax.axis_size("mp")
    dp_bits, mp_bits = _bits(n_dp), _bits(n_mp)
    rank = proj_in.shape[1]
    seq_len = activations.shape[2]
    ex_local = activations.shape[1]

    part_in = jnp.einsum("cesf,fr->cesr", activations, proj_in, preferred_element_type=jnp.float32)
    part_out = jnp.einsum("cesf,fr->cesr", out_grads, proj_out, preferred_element_type=jnp.float32)
    stacked = jnp.concatenate([part_in, part_out], axis=3)
    c, e, t, r = stacked.shape
    shares = lax.all_to_all(
        stacked.reshape(c, e, n_mp, t // n_mp, r), "mp", 2, 2, tiled=True
    )
    summed = shares.sum(2).astype(jnp.bfloat16)
    copies = jnp.broadcast_to(summed[:, :, None], (c, e, n_mp, t // n_mp, r))
    low = lax.all_to_all(copies, "mp", 2, 2, tiled=True).reshape(c, e, t, r)
    outer = jnp.einsum(
        "cesa,cesb->ecab", low[..., :rank], low[..., rank:], preferred_element_type=jnp.float32
    )
    outer = outer.reshape(ex_local, 2, rank * rank)
    query = (outer / jnp.sqrt(jnp.float32(seq_len))).astype(jnp.bfloat16)
    piece = _doubling_gather(query, "dp", n_dp, 0, list(reversed(range(dp_bits))))
    first = jnp.einsum("qk,rk->qr", piece[:, 0], store[0], preferred_element_type=jnp.float32)
    second = jnp.einsum("qk,rk->qr", piece[:, 1], store[1], preferred_element_type=jnp.float32)
    scores = ckpt_rate[0] * first + ckpt_rate[1] * second
    member = (store_group[:, None] == jnp.arange(GROUPS, dtype=jnp.int32)[None, :]).astype(
        jnp.float32
    )
    partial_totals = jnp.dot(scores, member, precision=lax.Precision.HIGHEST)
    copies = jnp.broadcast_to(partial_totals[None], (n_mp,) + partial_totals.shape)
    totals = lax.all_to_all(copies, "mp", 0, 0, tiled=True).sum(0)
    totals = _butterfly_sum(totals, "dp", n_dp, list(range(dp_bits)))

    def natural(x):
        x = x.reshape((2,) * dp_bits + (ex_local,) + x.shape[1:])
        perm = list(reversed(range(dp_bits))) + list(range(dp_bits, x.ndim))
        return jnp.transpose(x, perm).reshape((n_dp * ex_local,) + x.shape[dp_bits + 1 :])

    scores = natural(scores)
    store_rows = store.shape[1] * n_dp * n_mp
    group_scores = natural(totals) / jnp.sqrt(jnp.float32(store_rows) / jnp.float32(GROUPS))
    return (scores, group_scores)


def solution(mesh):
    placed = (
        P(None, "dp", None, "mp"),
        P(None, "dp", None, "mp"),
        P("mp", None),
        P("mp", None),
        P(None, ("dp", "mp"), None),
        P(),
        P(("dp", "mp")),
    )
    return jax.shard_map(
        shards, mesh=mesh, in_specs=placed, out_specs=(P(None, ("dp", "mp")), P()), check_vma=False
    )
```

```python
import jax
import jax.numpy as jnp
from jax import lax
from jax.sharding import PartitionSpec as P

GROUPS = 16


def _bits(n):
    return n.bit_length() - 1


def _swap(n, bit):
    return [(i, i ^ (1 << bit)) for i in range(n)]


def _halving_sum(x, axis, n, dim, order):
    me = lax.axis_index(axis)
    for bit in order:
        half = x.shape[dim] // 2
        upper = (me >> bit) & 1
        keep = lax.dynamic_slice_in_dim(x, upper * half, half, axis=dim)
        send = lax.dynamic_slice_in_dim(x, (1 - upper) * half, half, axis=dim)
        x = keep + lax.ppermute(send, axis, _swap(n, bit))
    return x


def _butterfly_sum(x, axis, n, order):
    for bit in order:
        x = x + lax.ppermute(x, axis, _swap(n, bit))
    return x


def _join(x, other, upper, dim):
    return jnp.where(upper, jnp.concatenate([other, x], dim), jnp.concatenate([x, other], dim))


def _doubling_gather(x, axis, n, dim, order):
    me = lax.axis_index(axis)
    for bit in order:
        upper = ((me >> bit) & 1) == 1
        x = _join(x, lax.ppermute(x, axis, _swap(n, bit)), upper, dim)
    return x


def shards(activations, out_grads, proj_in, proj_out, store, ckpt_rate, store_group):
    n_dp = lax.axis_size("dp")
    n_mp = lax.axis_size("mp")
    dp_bits, mp_bits = _bits(n_dp), _bits(n_mp)
    rank = proj_in.shape[1]
    seq_len = activations.shape[2]
    ex_local = activations.shape[1]

    part_in = jnp.einsum("cesf,fr->cesr", activations, proj_in, preferred_element_type=jnp.float32)
    part_out = jnp.einsum("cesf,fr->cesr", out_grads, proj_out, preferred_element_type=jnp.float32)
    stacked = jnp.concatenate([part_in, part_out], axis=3)
    c, e, t, r = stacked.shape
    shares = lax.all_to_all(
        stacked.reshape(c, e, n_mp, t // n_mp, r), "mp", 2, 2, tiled=True
    )
    summed = shares.sum(2).astype(jnp.bfloat16)
    copies = jnp.broadcast_to(summed[:, :, None], (c, e, n_mp, t // n_mp, r))
    low = lax.all_to_all(copies, "mp", 2, 2, tiled=True).reshape(c, e, t, r)
    outer = jnp.einsum(
        "cesa,cesb->ecab", low[..., :rank], low[..., rank:], preferred_element_type=jnp.float32
    )
    outer = outer.reshape(ex_local, 2, rank * rank)
    query = (outer / jnp.sqrt(jnp.float32(seq_len))).astype(jnp.bfloat16)
    member = (store_group[:, None] == jnp.arange(GROUPS, dtype=jnp.int32)[None, :]).astype(
        jnp.float32
    )

    def score(block):
        first = jnp.einsum("qk,rk->qr", block[:, 0], store[0], preferred_element_type=jnp.float32)
        second = jnp.einsum("qk,rk->qr", block[:, 1], store[1], preferred_element_type=jnp.float32)
        rows = ckpt_rate[0] * first + ckpt_rate[1] * second
        return rows, jnp.dot(rows, member, precision=lax.Precision.HIGHEST)

    me = lax.axis_index("dp")
    piece = query
    scores, partial_totals = score(query)
    for bit in reversed(range(dp_bits)):
        upper = ((me >> bit) & 1) == 1
        other = lax.ppermute(piece, "dp", _swap(n_dp, bit))
        if bit:
            piece = _join(piece, other, upper, 0)
        other_scores, other_totals = score(other)
        scores = _join(scores, other_scores, upper, 0)
        partial_totals = _join(partial_totals, other_totals, upper, 0)
    copies = jnp.broadcast_to(partial_totals[None], (n_mp,) + partial_totals.shape)
    totals = lax.all_to_all(copies, "mp", 0, 0, tiled=True).sum(0)
    totals = _butterfly_sum(totals, "dp", n_dp, list(range(dp_bits)))

    def natural(x):
        x = x.reshape((2,) * dp_bits + (ex_local,) + x.shape[1:])
        perm = list(reversed(range(dp_bits))) + list(range(dp_bits, x.ndim))
        return jnp.transpose(x, perm).reshape((n_dp * ex_local,) + x.shape[dp_bits + 1 :])

    scores = natural(scores)
    store_rows = store.shape[1] * n_dp * n_mp
    group_scores = natural(totals) / jnp.sqrt(jnp.float32(store_rows) / jnp.float32(GROUPS))
    return (scores, group_scores)


def solution(mesh):
    placed = (
        P(None, "dp", None, "mp"),
        P(None, "dp", None, "mp"),
        P("mp", None),
        P("mp", None),
        P(None, ("dp", "mp"), None),
        P(),
        P(("dp", "mp")),
    )
    return jax.shard_map(
        shards, mesh=mesh, in_specs=placed, out_specs=(P(None, ("dp", "mp")), P()), check_vma=False
    )
```

```python
import jax
import jax.numpy as jnp
from jax import lax
from jax.sharding import PartitionSpec as P

GROUPS = 16


def _bits(n):
    return n.bit_length() - 1


def _swap(n, bit):
    return [(i, i ^ (1 << bit)) for i in range(n)]


def _halving_sum(x, axis, n, dim, order):
    me = lax.axis_index(axis)
    for bit in order:
        half = x.shape[dim] // 2
        upper = (me >> bit) & 1
        keep = lax.dynamic_slice_in_dim(x, upper * half, half, axis=dim)
        send = lax.dynamic_slice_in_dim(x, (1 - upper) * half, half, axis=dim)
        x = keep + lax.ppermute(send, axis, _swap(n, bit))
    return x


def _butterfly_sum(x, axis, n, order):
    for bit in order:
        x = x + lax.ppermute(x, axis, _swap(n, bit))
    return x


def _join(x, other, upper, dim):
    return jnp.where(upper, jnp.concatenate([other, x], dim), jnp.concatenate([x, other], dim))


def _doubling_gather(x, axis, n, dim, order):
    me = lax.axis_index(axis)
    for bit in order:
        upper = ((me >> bit) & 1) == 1
        x = _join(x, lax.ppermute(x, axis, _swap(n, bit)), upper, dim)
    return x


def shards(activations, out_grads, proj_in, proj_out, store, ckpt_rate, store_group):
    n_dp = lax.axis_size("dp")
    n_mp = lax.axis_size("mp")
    dp_bits, mp_bits = _bits(n_dp), _bits(n_mp)
    rank = proj_in.shape[1]
    seq_len = activations.shape[2]
    ex_local = activations.shape[1]

    part_in = jnp.einsum("cesf,fr->cesr", activations, proj_in, preferred_element_type=jnp.float32)
    part_out = jnp.einsum("cesf,fr->cesr", out_grads, proj_out, preferred_element_type=jnp.float32)
    stacked = jnp.concatenate([part_in, part_out], axis=3)
    c, e, t, r = stacked.shape
    shares = lax.all_to_all(
        stacked.reshape(c, e, n_mp, t // n_mp, r), "mp", 2, 2, tiled=True
    )
    summed = shares.sum(2).astype(jnp.bfloat16)
    copies = jnp.broadcast_to(summed[:, :, None], (c, e, n_mp, t // n_mp, r))
    low = lax.all_to_all(copies, "mp", 2, 2, tiled=True).reshape(c, e, t, r)
    outer = jnp.einsum(
        "cesa,cesb->ecab", low[..., :rank], low[..., rank:], preferred_element_type=jnp.float32
    )
    outer = outer.reshape(ex_local, 2, rank * rank)
    query = (outer / jnp.sqrt(jnp.float32(seq_len))).astype(jnp.bfloat16)
    piece = _doubling_gather(query, "dp", n_dp, 0, list(reversed(range(dp_bits))))
    member = (store_group[:, None] == jnp.arange(GROUPS, dtype=jnp.int32)[None, :]).astype(
        jnp.bfloat16
    )
    group_rows = jnp.einsum("rg,crk->cgk", member, store, preferred_element_type=jnp.float32)
    by_ckpt = jnp.einsum(
        "qck,cgk->cqg", piece.astype(jnp.float32), group_rows, precision=lax.Precision.HIGHEST
    )
    partial_totals = ckpt_rate[0] * by_ckpt[0] + ckpt_rate[1] * by_ckpt[1]
    first = jnp.einsum("qk,rk->qr", piece[:, 0], store[0], preferred_element_type=jnp.float32)
    second = jnp.einsum("qk,rk->qr", piece[:, 1], store[1], preferred_element_type=jnp.float32)
    scores = ckpt_rate[0] * first + ckpt_rate[1] * second
    copies = jnp.broadcast_to(partial_totals[None], (n_mp,) + partial_totals.shape)
    totals = lax.all_to_all(copies, "mp", 0, 0, tiled=True).sum(0)
    totals = _butterfly_sum(totals, "dp", n_dp, list(range(dp_bits)))

    def natural(x):
        x = x.reshape((2,) * dp_bits + (ex_local,) + x.shape[1:])
        perm = list(reversed(range(dp_bits))) + list(range(dp_bits, x.ndim))
        return jnp.transpose(x, perm).reshape((n_dp * ex_local,) + x.shape[dp_bits + 1 :])

    scores = natural(scores)
    store_rows = store.shape[1] * n_dp * n_mp
    group_scores = natural(totals) / jnp.sqrt(jnp.float32(store_rows) / jnp.float32(GROUPS))
    return (scores, group_scores)


def solution(mesh):
    placed = (
        P(None, "dp", None, "mp"),
        P(None, "dp", None, "mp"),
        P("mp", None),
        P("mp", None),
        P(None, ("dp", "mp"), None),
        P(),
        P(("dp", "mp")),
    )
    return jax.shard_map(
        shards, mesh=mesh, in_specs=placed, out_specs=(P(None, ("dp", "mp")), P()), check_vma=False
    )
```

```python
import jax
import jax.numpy as jnp
from jax import lax
from jax.sharding import PartitionSpec as P

GROUPS = 16


def _bits(n):
    return n.bit_length() - 1


def _swap(n, bit):
    return [(i, i ^ (1 << bit)) for i in range(n)]


def _halving_sum(x, axis, n, dim, order):
    me = lax.axis_index(axis)
    for bit in order:
        half = x.shape[dim] // 2
        upper = (me >> bit) & 1
        keep = lax.dynamic_slice_in_dim(x, upper * half, half, axis=dim)
        send = lax.dynamic_slice_in_dim(x, (1 - upper) * half, half, axis=dim)
        x = keep + lax.ppermute(send, axis, _swap(n, bit))
    return x


def _butterfly_sum(x, axis, n, order):
    for bit in order:
        x = x + lax.ppermute(x, axis, _swap(n, bit))
    return x


def _join(x, other, upper, dim):
    return jnp.where(upper, jnp.concatenate([other, x], dim), jnp.concatenate([x, other], dim))


def _doubling_gather(x, axis, n, dim, order):
    me = lax.axis_index(axis)
    for bit in order:
        upper = ((me >> bit) & 1) == 1
        x = _join(x, lax.ppermute(x, axis, _swap(n, bit)), upper, dim)
    return x


def shards(activations, out_grads, proj_in, proj_out, store, ckpt_rate, store_group):
    n_dp = lax.axis_size("dp")
    n_mp = lax.axis_size("mp")
    dp_bits, mp_bits = _bits(n_dp), _bits(n_mp)
    rank = proj_in.shape[1]
    seq_len = activations.shape[2]
    ex_local = activations.shape[1]

    part_in = jnp.einsum("cesf,fr->cesr", activations, proj_in, preferred_element_type=jnp.float32)
    part_out = jnp.einsum("cesf,fr->cesr", out_grads, proj_out, preferred_element_type=jnp.float32)
    stacked = jnp.concatenate([part_in, part_out], axis=3)
    c, e, t, r = stacked.shape
    shares = lax.all_to_all(
        stacked.reshape(c, e, n_mp, t // n_mp, r), "mp", 2, 2, tiled=True
    )
    summed = shares.sum(2).astype(jnp.bfloat16)
    copies = jnp.broadcast_to(summed[:, :, None], (c, e, n_mp, t // n_mp, r))
    low = lax.all_to_all(copies, "mp", 2, 2, tiled=True).reshape(c, e, t, r)
    outer = jnp.einsum(
        "cesa,cesb->ecab", low[..., :rank], low[..., rank:], preferred_element_type=jnp.float32
    )
    outer = outer.reshape(ex_local, 2, rank * rank)
    query = (outer / jnp.sqrt(jnp.float32(seq_len))).astype(jnp.bfloat16)
    piece = _doubling_gather(query, "dp", n_dp, 0, list(reversed(range(dp_bits))))
    by_ckpt = jnp.einsum("qck,crk->cqr", piece, store, preferred_element_type=jnp.float32)
    scores = ckpt_rate[0] * by_ckpt[0] + ckpt_rate[1] * by_ckpt[1]
    member = (store_group[:, None] == jnp.arange(GROUPS, dtype=jnp.int32)[None, :]).astype(
        jnp.float32
    )
    partial_totals = jnp.dot(scores, member, precision=lax.Precision.HIGHEST)
    copies = jnp.broadcast_to(partial_totals[None], (n_mp,) + partial_totals.shape)
    totals = lax.all_to_all(copies, "mp", 0, 0, tiled=True).sum(0)
    totals = _butterfly_sum(totals, "dp", n_dp, list(range(dp_bits)))

    def natural(x):
        x = x.reshape((2,) * dp_bits + (ex_local,) + x.shape[1:])
        perm = list(reversed(range(dp_bits))) + list(range(dp_bits, x.ndim))
        return jnp.transpose(x, perm).reshape((n_dp * ex_local,) + x.shape[dp_bits + 1 :])

    scores = natural(scores)
    store_rows = store.shape[1] * n_dp * n_mp
    group_scores = natural(totals) / jnp.sqrt(jnp.float32(store_rows) / jnp.float32(GROUPS))
    return (scores, group_scores)


def solution(mesh):
    placed = (
        P(None, "dp", None, "mp"),
        P(None, "dp", None, "mp"),
        P("mp", None),
        P("mp", None),
        P(None, ("dp", "mp"), None),
        P(),
        P(("dp", "mp")),
    )
    return jax.shard_map(
        shards, mesh=mesh, in_specs=placed, out_specs=(P(None, ("dp", "mp")), P()), check_vma=False
    )
```

```python
import jax
import jax.numpy as jnp
from jax import lax
from jax.sharding import PartitionSpec as P

GROUPS = 16


def _bits(n):
    return n.bit_length() - 1


def _swap(n, bit):
    return [(i, i ^ (1 << bit)) for i in range(n)]


def _halving_sum(x, axis, n, dim, order):
    me = lax.axis_index(axis)
    for bit in order:
        half = x.shape[dim] // 2
        upper = (me >> bit) & 1
        keep = lax.dynamic_slice_in_dim(x, upper * half, half, axis=dim)
        send = lax.dynamic_slice_in_dim(x, (1 - upper) * half, half, axis=dim)
        x = keep + lax.ppermute(send, axis, _swap(n, bit))
    return x


def _butterfly_sum(x, axis, n, order):
    for bit in order:
        x = x + lax.ppermute(x, axis, _swap(n, bit))
    return x


def _join(x, other, upper, dim):
    return jnp.where(upper, jnp.concatenate([other, x], dim), jnp.concatenate([x, other], dim))


def _doubling_gather(x, axis, n, dim, order):
    me = lax.axis_index(axis)
    for bit in order:
        upper = ((me >> bit) & 1) == 1
        x = _join(x, lax.ppermute(x, axis, _swap(n, bit)), upper, dim)
    return x


def _dp_steps(n):
    bits = _bits(n)
    steps = []
    lo = bits - 2
    while lo >= 1:
        steps += [(3 << lo, (lo + 1,)), (1 << lo, (lo, lo + 1))]
        lo -= 2
    for b in reversed(range(lo + 2)):
        steps.append((1 << b, (b,)))
    return steps


def _natural_rows(steps, n, ex_local):
    held = [[d] for d in range(n)]
    for mask, upper_bits in steps:
        held = [
            held[d ^ mask] + held[d] if sum(d >> b for b in upper_bits) & 1 else held[d] + held[d ^ mask]
            for d in range(n)
        ]
    order = held[0]
    assert all(h == order for h in held) and sorted(order) == list(range(n))
    where = {d: p for p, d in enumerate(order)}
    return [where[d] * ex_local + e for d in range(n) for e in range(ex_local)]


def shards(activations, out_grads, proj_in, proj_out, store, ckpt_rate, store_group):
    n_dp = lax.axis_size("dp")
    n_mp = lax.axis_size("mp")
    dp_bits, mp_bits = _bits(n_dp), _bits(n_mp)
    rank = proj_in.shape[1]
    seq_len = activations.shape[2]
    ex_local = activations.shape[1]

    part_in = jnp.einsum("cesf,fr->cesr", activations, proj_in, preferred_element_type=jnp.float32)
    part_out = jnp.einsum("cesf,fr->cesr", out_grads, proj_out, preferred_element_type=jnp.float32)
    stacked = jnp.concatenate([part_in, part_out], axis=3)
    c, e, t, r = stacked.shape
    shares = lax.all_to_all(
        stacked.reshape(c, e, n_mp, t // n_mp, r), "mp", 2, 2, tiled=True
    )
    summed = shares.sum(2).astype(jnp.bfloat16)
    copies = jnp.broadcast_to(summed[:, :, None], (c, e, n_mp, t // n_mp, r))
    low = lax.all_to_all(copies, "mp", 2, 2, tiled=True).reshape(c, e, t, r)
    outer = jnp.einsum(
        "cesa,cesb->ecab", low[..., :rank], low[..., rank:], preferred_element_type=jnp.float32
    )
    outer = outer.reshape(ex_local, 2, rank * rank)
    query = (outer / jnp.sqrt(jnp.float32(seq_len))).astype(jnp.bfloat16)
    steps = _dp_steps(n_dp)
    me = lax.axis_index("dp")
    piece = query
    for mask, upper_bits in steps:
        upper = (sum((me >> b) for b in upper_bits) & 1) == 1
        other = lax.ppermute(piece, "dp", [(i, i ^ mask) for i in range(n_dp)])
        piece = _join(piece, other, upper, 0)
    first = jnp.einsum("qk,rk->qr", piece[:, 0], store[0], preferred_element_type=jnp.float32)
    second = jnp.einsum("qk,rk->qr", piece[:, 1], store[1], preferred_element_type=jnp.float32)
    scores = ckpt_rate[0] * first + ckpt_rate[1] * second
    member = (store_group[:, None] == jnp.arange(GROUPS, dtype=jnp.int32)[None, :]).astype(
        jnp.float32
    )
    partial_totals = jnp.dot(scores, member, precision=lax.Precision.HIGHEST)
    copies = jnp.broadcast_to(partial_totals[None], (n_mp,) + partial_totals.shape)
    totals = lax.all_to_all(copies, "mp", 0, 0, tiled=True).sum(0)
    for mask, _ in reversed(steps):
        totals = totals + lax.ppermute(totals, "dp", [(i, i ^ mask) for i in range(n_dp)])

    rows = jnp.asarray(_natural_rows(steps, n_dp, ex_local), jnp.int32)

    def natural(x):
        return jnp.take(x, rows, axis=0)

    scores = natural(scores)
    store_rows = store.shape[1] * n_dp * n_mp
    group_scores = natural(totals) / jnp.sqrt(jnp.float32(store_rows) / jnp.float32(GROUPS))
    return (scores, group_scores)


def solution(mesh):
    placed = (
        P(None, "dp", None, "mp"),
        P(None, "dp", None, "mp"),
        P("mp", None),
        P("mp", None),
        P(None, ("dp", "mp"), None),
        P(),
        P(("dp", "mp")),
    )
    return jax.shard_map(
        shards, mesh=mesh, in_specs=placed, out_specs=(P(None, ("dp", "mp")), P()), check_vma=False
    )
```
